256 devices in a mesh: wide: 64 (over z, x, y_lo), narrow: 4 (over y_hi, core).
Axes of the slice: x: 4, y: 4 (y_hi: 2, y_lo: 2; y = y_hi * 2 + y_lo), z: 8, core: 2. Of those that a mesh axis runs over, the one named last changes fastest.
Arguments:
- density: bfloat16 [8192, 8, 128], P(('wide', 'narrow')), may hold values from -6 to 6
- basis: bfloat16 [8192, 64, 128], P(('wide', 'narrow')), may hold values from -0.5 to 0.5
- near_list: int32 [8192, 6], P(('wide', 'narrow')), may hold values from 0 to 8191, as said below
- near_blocks: bfloat16 [8192, 6, 128, 128], P(('wide', 'narrow')), may hold values from -0.21875 to 0.21875
- far_leaf: int32 [8192, 6], P(('wide', 'narrow')), may hold values from 0 to 8191, as said below
- leaf_coupling: bfloat16 [8192, 64, 384], P(('wide', 'narrow')), may hold values from -0.3125 to 0.3125
- transfer: bfloat16 [1024, 64, 512], P(('wide', 'narrow')), may hold values from -0.75 to 0.75
- far_coarse: int32 [1024, 8], P(('wide', 'narrow')), may hold values from 0 to 1023
- coarse_coupling: bfloat16 [1024, 64, 512], P(('wide', 'narrow')), may hold values from -0.25 to 0.25
Outputs:
- potential: bfloat16 [8192, 8, 128], P(('wide', 'narrow'))
The draws below stay inside these ranges and needn't reach their ends.
Inputs may be any that keep to these rules, and one draw needn't show every extreme that they name: `near_list`: every entry lies within 32 leaves of its own leaf l; the first entry is l itself. `far_leaf`: every entry lies within 32 leaves of its own leaf.
All inputs are finite; a program needn't handle non-finite values.
Results may differ from the reference program's by a relative error of at most 0.0066.
Values may be sent and summed in bfloat16 or wider, within the bound.
No kernel may reach another device: no remote copies, remote signals or barrier semaphores. Data moves between devices by JAX's collectives and lax.ppermute only.
A program may use at most 64 MiB of HBM per device.

```python
import jax
import jax.numpy as jnp
from jax import lax

LEAF = 128
RANK = 64
RHS = 8
NEAR = 6
FAR_LEAF = 6
FAR_COARSE = 8
KIDS = 8
LEAF_DEV = 32
LEAVES = 8192
BOX_DEV = 4
BOXES = 1024


def draw_near_list(key, part):
    offsets = jax.random.randint(key, (LEAVES, NEAR), -LEAF_DEV, LEAF_DEV + 1)
    column = jnp.arange(NEAR, dtype=jnp.int32)[None, :]
    offsets = jnp.where(column == 0, 0, offsets)
    leaves = jnp.arange(LEAVES, dtype=jnp.int32)[:, None]
    return jnp.clip(leaves + offsets, 0, LEAVES - 1).astype(jnp.int32)


def draw_far_leaf(key, part):
    offsets = jax.random.randint(jax.random.fold_in(key, 7), (LEAVES, FAR_LEAF), -LEAF_DEV, LEAF_DEV + 1)
    leaves = jnp.arange(LEAVES, dtype=jnp.int32)[:, None]
    return jnp.clip(leaves + offsets, 0, LEAVES - 1).astype(jnp.int32)


def draw_far_coarse(key, part):
    return jax.random.randint(jax.random.fold_in(key, 11), (BOXES, FAR_COARSE), 0, BOXES).astype(jnp.int32)


def block_levels(rng, extent, shards, smallest, top_value):
    loudness = 1.0
    for dim, blocks in shards:
        draws = jax.random.uniform(jax.random.fold_in(jax.random.fold_in(rng, 6), dim), (blocks,), jnp.float32, smallest / len(shards), top_value / len(shards))
        loudness = loudness * jnp.repeat(jnp.exp(draws), extent[dim] // blocks).reshape((-1,) + (1,) * (len(extent) - 1 - dim))
    return loudness


def gaussian(own_key, dims, scale, limit, shards=(), kind=jnp.bfloat16):
    drawn = jax.random.normal(own_key, dims, jnp.float32) * scale
    if len(shards) > 0:
        drawn = block_levels(own_key, dims, shards, -0.22, 0.18) * drawn
    return jnp.clip(drawn, min=-limit, max=limit).astype(kind)


def setup_inputs(seed: int = 0) -> dict:
    keys = jax.random.split(jax.random.key(seed), 10)
    return {
        "density": gaussian(keys[0], (LEAVES, RHS, LEAF), 1.0, 6.0, ((0, 256),)),
        "basis": gaussian(keys[1], (LEAVES, RANK, LEAF), LEAF ** -0.5, 0.5, ((0, 256),)),
        "near_list": draw_near_list(jax.random.fold_in(keys[9], 71), 0),
        "near_blocks": gaussian(keys[3], (LEAVES, NEAR, LEAF, LEAF), (LEAF * NEAR) ** -0.5, 0.21875, ((0, 256),)),
        "far_leaf": draw_far_leaf(jax.random.fold_in(keys[9], 71), 0),
        "leaf_coupling": gaussian(keys[5], (LEAVES, RANK, FAR_LEAF * RANK), (RANK * FAR_LEAF) ** -0.5, 0.3125, ((0, 256),)),
        "transfer": gaussian(keys[6], (BOXES, RANK, KIDS * RANK), RANK ** -0.5, 0.75, ((0, 256),)),
        "far_coarse": draw_far_coarse(jax.random.fold_in(keys[9], 71), 0),
        "coarse_coupling": gaussian(keys[8], (BOXES, RANK, FAR_COARSE * RANK), (RANK * FAR_COARSE) ** -0.5, 0.25, ((0, 256),)),
    }


def upward(items):
    dens, base, trans = items
    skeleton = jnp.einsum('lrp,lkp->lrk', dens.astype(jnp.float32), base.astype(jnp.float32)).astype(jnp.bfloat16)
    children = skeleton.reshape(BOX_DEV, KIDS, RHS, RANK)
    coarse = jnp.einsum('ckim,cirm->crk', trans.reshape(BOX_DEV, RANK, KIDS, RANK).astype(jnp.float32), children.astype(jnp.float32)).astype(jnp.bfloat16)
    return skeleton, coarse


def reference(density, basis, near_list, near_blocks, far_leaf, leaf_coupling, transfer, far_coarse, coarse_coupling):
    blocks = LEAVES // LEAF_DEV
    skeleton, coarse = lax.map(upward, (density.reshape(blocks, LEAF_DEV, RHS, LEAF), basis.reshape(blocks, LEAF_DEV, RANK, LEAF), transfer.reshape(blocks, BOX_DEV, RANK, KIDS * RANK)))
    skeleton = skeleton.reshape(LEAVES, RHS, RANK)
    coarse = coarse.reshape(BOXES, RHS, RANK)

    def downward(items):
        base, nears, dense, fars, leaf_cpl, trans, coarse_ids, coarse_cpl = items
        near_rows = density[nears].astype(jnp.float32)
        near_part = jnp.einsum('ljpq,ljrq->lrp', dense.astype(jnp.float32), near_rows)
        far_skels = skeleton[fars].astype(jnp.float32)
        leaf_far = jnp.einsum('lkjm,ljrm->lrk', leaf_cpl.reshape(LEAF_DEV, RANK, FAR_LEAF, RANK).astype(jnp.float32), far_skels)
        coarse_skels = coarse[coarse_ids].astype(jnp.float32)
        coarse_field = jnp.einsum('ckjm,cjrm->crk', coarse_cpl.reshape(BOX_DEV, RANK, FAR_COARSE, RANK).astype(jnp.float32), coarse_skels).astype(jnp.bfloat16)
        descended = jnp.einsum('ckim,crk->cirm', trans.reshape(BOX_DEV, RANK, KIDS, RANK).astype(jnp.float32), coarse_field.astype(jnp.float32)).reshape(LEAF_DEV, RHS, RANK)
        local_field = (leaf_far + descended).astype(jnp.bfloat16)
        total = jnp.einsum('lrk,lkp->lrp', local_field.astype(jnp.float32), base.astype(jnp.float32)) + near_part
        return total.astype(jnp.bfloat16)

    result = lax.map(downward, (
        basis.reshape(blocks, LEAF_DEV, RANK, LEAF),
        near_list.reshape(blocks, LEAF_DEV, NEAR),
        near_blocks.reshape(blocks, LEAF_DEV, NEAR, LEAF, LEAF),
        far_leaf.reshape(blocks, LEAF_DEV, FAR_LEAF),
        leaf_coupling.reshape(blocks, LEAF_DEV, RANK, FAR_LEAF * RANK),
        transfer.reshape(blocks, BOX_DEV, RANK, KIDS * RANK),
        far_coarse.reshape(blocks, BOX_DEV, FAR_COARSE),
        coarse_coupling.reshape(blocks, BOX_DEV, RANK, FAR_COARSE * RANK)))
    return result.reshape(LEAVES, RHS, LEAF)
```

```python
import jax
import jax.numpy as jnp
from jax import lax
from jax.sharding import Mesh, PartitionSpec as P

ALL = ("z", "x", "y_lo", "y_hi", "core")
STAGES = (("z",), ("x", "y_lo", "y_hi"), ("core",))


def with_halo(block, sides, width):
    for axis, dim in sides:
        count = lax.axis_size(axis)
        forward = [(i, i + 1) for i in range(count - 1)]
        backward = [(target, source) for source, target in forward]
        low = lax.ppermute(
            lax.slice_in_dim(block, block.shape[dim] - width, None, axis=dim), axis, forward
        )
        high = lax.ppermute(lax.slice_in_dim(block, 0, width, axis=dim), axis, backward)
        block = jnp.concatenate([low, block, high], axis=dim)
    return block


def body(
    density,
    basis,
    near_list,
    near_blocks,
    far_leaf,
    leaf_coupling,
    transfer,
    far_coarse,
    coarse_coupling,
):
    leaf_count, rhs_count, leaf_width = density.shape
    rank_width = basis.shape[1]
    box_count = transfer.shape[0]
    child_count = leaf_count // box_count
    far_count = far_leaf.shape[1]
    coarse_count = far_coarse.shape[1]
    skeleton = jnp.einsum(
        "lrp,lkp->lrk", density, basis, preferred_element_type=jnp.float32
    ).astype(jnp.bfloat16)
    children = skeleton.reshape(box_count, child_count, rhs_count, rank_width)
    coarse = jnp.einsum(
        "ckim,cirm->crk",
        transfer.reshape(box_count, rank_width, child_count, rank_width),
        children,
        preferred_element_type=jnp.float32,
    ).astype(jnp.bfloat16)
    coarse_flat = coarse.reshape(box_count, rhs_count * rank_width)
    everything = coarse_flat
    for axes in STAGES:
        n = lax.axis_size(axes)
        spread = jnp.broadcast_to(everything[None], (n,) + everything.shape)
        everything = lax.all_to_all(spread, axes, 0, 0, tiled=False).reshape(
            (n * everything.shape[0],) + everything.shape[1:]
        )
    offset_base = lax.axis_index(ALL) * leaf_count - leaf_count
    density_flat = density.reshape(leaf_count, rhs_count * leaf_width)
    skeleton_flat = skeleton.reshape(leaf_count, rhs_count * rank_width)
    density_padded = with_halo(density_flat, ((ALL, 0),), leaf_count)
    skeleton_padded = with_halo(skeleton_flat, ((ALL, 0),), leaf_count)
    near_rows = jnp.take(density_padded, near_list - offset_base, axis=0).reshape(
        leaf_count, near_list.shape[1], rhs_count, leaf_width
    )
    near_part = jnp.einsum(
        "ljpq,ljrq->lrp", near_blocks, near_rows, preferred_element_type=jnp.float32
    )
    far_skels = jnp.take(skeleton_padded, far_leaf - offset_base, axis=0).reshape(
        leaf_count, far_count, rhs_count, rank_width
    )
    leaf_far = jnp.einsum(
        "lkjm,ljrm->lrk",
        leaf_coupling.reshape(leaf_count, rank_width, far_count, rank_width),
        far_skels,
        preferred_element_type=jnp.float32,
    )
    sizes = [lax.axis_size(a) for a in ALL]
    owner, slot = far_coarse // box_count, far_coarse % box_count
    coords = []
    for size in reversed(sizes):
        coords.append(owner % size)
        owner = owner // size
    coords = dict(zip(reversed(ALL), coords))
    position = 0
    for axes in reversed(STAGES):
        for a in axes:
            position = position * lax.axis_size(a) + coords[a]
    coarse_skels = jnp.take(everything, position * box_count + slot, axis=0).reshape(
        box_count, coarse_count, rhs_count, rank_width
    )
    coarse_field = jnp.einsum(
        "ckjm,cjrm->crk",
        coarse_coupling.reshape(box_count, rank_width, coarse_count, rank_width),
        coarse_skels,
        preferred_element_type=jnp.float32,
    ).astype(jnp.bfloat16)
    descended = jnp.einsum(
        "ckim,crk->cirm",
        transfer.reshape(box_count, rank_width, child_count, rank_width),
        coarse_field,
        preferred_element_type=jnp.float32,
    ).reshape(leaf_count, rhs_count, rank_width)
    local_field = (leaf_far + descended).astype(jnp.bfloat16)
    total = (
        jnp.einsum("lrk,lkp->lrp", local_field, basis, preferred_element_type=jnp.float32)
        + near_part
    )
    return total.astype(jnp.bfloat16)


def solution(mesh):
    assert tuple(mesh.shape.values()) == (64, 4)
    grid = Mesh(mesh.devices.reshape(8, 4, 2, 2, 2), ALL)
    return jax.shard_map(
        body,
        mesh=grid,
        in_specs=(
            P(ALL, None, None),
            P(ALL, None, None),
            P(ALL, None),
            P(ALL, None, None, None),
            P(ALL, None),
            P(ALL, None, None),
            P(ALL, None, None),
            P(ALL, None),
            P(ALL, None, None),
        ),
        out_specs=P(ALL, None, None),
        check_vma=False,
    )
```

```python
import jax
import jax.numpy as jnp
from jax import lax
from jax.sharding import Mesh, PartitionSpec as P

ALL = ("z", "x", "y_lo", "y_hi", "core")
STAGES = (("z",), ("x", "y_lo", "y_hi"))
PAIR = "core"


def with_halo(block, sides, width):
    for axis, dim in sides:
        count = lax.axis_size(axis)
        forward = [(i, i + 1) for i in range(count - 1)]
        backward = [(target, source) for source, target in forward]
        low = lax.ppermute(
            lax.slice_in_dim(block, block.shape[dim] - width, None, axis=dim), axis, forward
        )
        high = lax.ppermute(lax.slice_in_dim(block, 0, width, axis=dim), axis, backward)
        block = jnp.concatenate([low, block, high], axis=dim)
    return block


def body(
    density,
    basis,
    near_list,
    near_blocks,
    far_leaf,
    leaf_coupling,
    transfer,
    far_coarse,
    coarse_coupling,
):
    leaf_count, rhs_count, leaf_width = density.shape
    rank_width = basis.shape[1]
    box_count = transfer.shape[0]
    child_count = leaf_count // box_count
    far_count = far_leaf.shape[1]
    coarse_count = far_coarse.shape[1]
    skeleton = jnp.einsum(
        "lrp,lkp->lrk", density, basis, preferred_element_type=jnp.float32
    ).astype(jnp.bfloat16)
    children = skeleton.reshape(box_count, child_count, rhs_count, rank_width)
    coarse = jnp.einsum(
        "ckim,cirm->crk",
        transfer.reshape(box_count, rank_width, child_count, rank_width),
        children,
        preferred_element_type=jnp.float32,
    ).astype(jnp.bfloat16)
    coarse_flat = coarse.reshape(box_count, rhs_count * rank_width)
    everything = coarse_flat
    for axes in STAGES:
        n = lax.axis_size(axes)
        spread = jnp.broadcast_to(everything[None], (n,) + everything.shape)
        everything = lax.all_to_all(spread, axes, 0, 0, tiled=False).reshape(
            (n * everything.shape[0],) + everything.shape[1:]
        )
    partner = lax.ppermute(everything, PAIR, [(0, 1), (1, 0)])
    everything = jnp.concatenate([everything, partner], axis=0)
    offset_base = lax.axis_index(ALL) * leaf_count - leaf_count
    density_flat = density.reshape(leaf_count, rhs_count * leaf_width)
    skeleton_flat = skeleton.reshape(leaf_count, rhs_count * rank_width)
    both_padded = with_halo(
        jnp.concatenate([density_flat, skeleton_flat], axis=1), ((ALL, 0),), leaf_count
    )
    density_padded = both_padded[:, : density_flat.shape[1]]
    skeleton_padded = both_padded[:, density_flat.shape[1] :]
    near_rows = jnp.take(density_padded, near_list - offset_base, axis=0).reshape(
        leaf_count, near_list.shape[1], rhs_count, leaf_width
    )
    near_part = jnp.einsum(
        "ljpq,ljrq->lrp", near_blocks, near_rows, preferred_element_type=jnp.float32
    )
    far_skels = jnp.take(skeleton_padded, far_leaf - offset_base, axis=0).reshape(
        leaf_count, far_count, rhs_count, rank_width
    )
    leaf_far = jnp.einsum(
        "lkjm,ljrm->lrk",
        leaf_coupling.reshape(leaf_count, rank_width, far_count, rank_width),
        far_skels,
        preferred_element_type=jnp.float32,
    )
    sizes = [lax.axis_size(a) for a in ALL]
    owner, slot = far_coarse // box_count, far_coarse % box_count
    coords = []
    for size in reversed(sizes):
        coords.append(owner % size)
        owner = owner // size
    coords = dict(zip(reversed(ALL), coords))
    position = (coords[PAIR] != lax.axis_index(PAIR)).astype(jnp.int32)
    for axes in reversed(STAGES):
        for a in axes:
            position = position * lax.axis_size(a) + coords[a]
    coarse_skels = jnp.take(everything, position * box_count + slot, axis=0).reshape(
        box_count, coarse_count, rhs_count, rank_width
    )
    coarse_field = jnp.einsum(
        "ckjm,cjrm->crk",
        coarse_coupling.reshape(box_count, rank_width, coarse_count, rank_width),
        coarse_skels,
        preferred_element_type=jnp.float32,
    ).astype(jnp.bfloat16)
    descended = jnp.einsum(
        "ckim,crk->cirm",
        transfer.reshape(box_count, rank_width, child_count, rank_width),
        coarse_field,
        preferred_element_type=jnp.float32,
    ).reshape(leaf_count, rhs_count, rank_width)
    local_field = (leaf_far + descended).astype(jnp.bfloat16)
    total = (
        jnp.einsum("lrk,lkp->lrp", local_field, basis, preferred_element_type=jnp.float32)
        + near_part
    )
    return total.astype(jnp.bfloat16)


def solution(mesh):
    assert tuple(mesh.shape.values()) == (64, 4)
    grid = Mesh(mesh.devices.reshape(8, 4, 2, 2, 2), ALL)
    return jax.shard_map(
        body,
        mesh=grid,
        in_specs=(
            P(ALL, None, None),
            P(ALL, None, None),
            P(ALL, None),
            P(ALL, None, None, None),
            P(ALL, None),
            P(ALL, None, None),
            P(ALL, None, None),
            P(ALL, None),
            P(ALL, None, None),
        ),
        out_specs=P(ALL, None, None),
        check_vma=False,
    )
```

```python
import jax
import jax.numpy as jnp
from jax import lax
from jax.sharding import Mesh, PartitionSpec as P

ALL = ("z", "x", "y_lo", "y_hi", "core")
STAGES = (("z",), ("x", "y_lo", "y_hi"))
PAIR = "core"


def with_halo(block, sides, width):
    for axis, dim in sides:
        count = lax.axis_size(axis)
        forward = [(i, i + 1) for i in range(count - 1)]
        backward = [(target, source) for source, target in forward]
        low = lax.ppermute(
            lax.slice_in_dim(block, block.shape[dim] - width, None, axis=dim), axis, forward
        )
        high = lax.ppermute(lax.slice_in_dim(block, 0, width, axis=dim), axis, backward)
        block = jnp.concatenate([low, block, high], axis=dim)
    return block


def side_by_side(parts):
    n, j, r, m = parts.shape
    return parts.transpose(0, 2, 1, 3).reshape(n, r, j * m)


def body(
    density,
    basis,
    near_list,
    near_blocks,
    far_leaf,
    leaf_coupling,
    transfer,
    far_coarse,
    coarse_coupling,
):
    leaf_count, rhs_count, leaf_width = density.shape
    rank_width = basis.shape[1]
    box_count = transfer.shape[0]
    child_count = leaf_count // box_count
    far_count = far_leaf.shape[1]
    coarse_count = far_coarse.shape[1]
    skeleton = jnp.einsum(
        "lrp,lkp->lrk", density, basis, preferred_element_type=jnp.float32
    ).astype(jnp.bfloat16)
    children = skeleton.reshape(box_count, child_count, rhs_count, rank_width)
    coarse = jnp.einsum(
        "ckq,crq->crk", transfer, side_by_side(children), preferred_element_type=jnp.float32
    ).astype(jnp.bfloat16)
    coarse_flat = coarse.reshape(box_count, rhs_count * rank_width)
    everything = coarse_flat
    for axes in STAGES:
        n = lax.axis_size(axes)
        spread = jnp.broadcast_to(everything[None], (n,) + everything.shape)
        everything = lax.all_to_all(spread, axes, 0, 0, tiled=False).reshape(
            (n * everything.shape[0],) + everything.shape[1:]
        )
    partner = lax.ppermute(everything, PAIR, [(0, 1), (1, 0)])
    everything = jnp.concatenate([everything, partner], axis=0)
    offset_base = lax.axis_index(ALL) * leaf_count - leaf_count
    density_flat = density.reshape(leaf_count, rhs_count * leaf_width)
    skeleton_flat = skeleton.reshape(leaf_count, rhs_count * rank_width)
    both_padded = with_halo(
        jnp.concatenate([density_flat, skeleton_flat], axis=1), ((ALL, 0),), leaf_count
    )
    density_padded = both_padded[:, : density_flat.shape[1]]
    skeleton_padded = both_padded[:, density_flat.shape[1] :]
    near_rows = jnp.take(density_padded, near_list - offset_base, axis=0).reshape(
        leaf_count, near_list.shape[1], rhs_count, leaf_width
    )
    near_part = jnp.einsum(
        "ljpq,ljrq->lrp", near_blocks, near_rows, preferred_element_type=jnp.float32
    )
    far_skels = jnp.take(skeleton_padded, far_leaf - offset_base, axis=0).reshape(
        leaf_count, far_count, rhs_count, rank_width
    )
    leaf_far = jnp.einsum(
        "lkq,lrq->lrk", leaf_coupling, side_by_side(far_skels), preferred_element_type=jnp.float32
    )
    sizes = [lax.axis_size(a) for a in ALL]
    owner, slot = far_coarse // box_count, far_coarse % box_count
    coords = []
    for size in reversed(sizes):
        coords.append(owner % size)
        owner = owner // size
    coords = dict(zip(reversed(ALL), coords))
    position = (coords[PAIR] != lax.axis_index(PAIR)).astype(jnp.int32)
    for axes in reversed(STAGES):
        for a in axes:
            position = position * lax.axis_size(a) + coords[a]
    coarse_skels = jnp.take(everything, position * box_count + slot, axis=0).reshape(
        box_count, coarse_count, rhs_count, rank_width
    )
    coarse_field = jnp.einsum(
        "ckq,crq->crk", coarse_coupling, side_by_side(coarse_skels), preferred_element_type=jnp.float32
    ).astype(jnp.bfloat16)
    descended = jnp.einsum(
        "crk,ckq->crq", coarse_field, transfer, preferred_element_type=jnp.float32
    )
    descended = (
        descended.reshape(box_count, rhs_count, child_count, rank_width)
        .transpose(0, 2, 1, 3)
        .reshape(leaf_count, rhs_count, rank_width)
    )
    local_field = (leaf_far + descended).astype(jnp.bfloat16)
    total = (
        jnp.einsum("lrk,lkp->lrp", local_field, basis, preferred_element_type=jnp.float32)
        + near_part
    )
    return total.astype(jnp.bfloat16)


def solution(mesh):
    assert tuple(mesh.shape.values()) == (64, 4)
    grid = Mesh(mesh.devices.reshape(8, 4, 2, 2, 2), ALL)
    return jax.shard_map(
        body,
        mesh=grid,
        in_specs=(
            P(ALL, None, None),
            P(ALL, None, None),
            P(ALL, None),
            P(ALL, None, None, None),
            P(ALL, None),
            P(ALL, None, None),
            P(ALL, None, None),
            P(ALL, None),
            P(ALL, None, None),
        ),
        out_specs=P(ALL, None, None),
        check_vma=False,
    )
```

```python
import jax
import jax.numpy as jnp
from jax import lax
from jax.sharding import Mesh, PartitionSpec as P

ALL = ("z", "x", "y_lo", "y_hi", "core")
STAGES = (("z",), ("x", "y_lo", "y_hi"))
PAIR = "core"


def with_halo(block, sides, width):
    for axis, dim in sides:
        count = lax.axis_size(axis)
        forward = [(i, i + 1) for i in range(count - 1)]
        backward = [(target, source) for source, target in forward]
        low = lax.ppermute(
            lax.slice_in_dim(block, block.shape[dim] - width, None, axis=dim), axis, forward
        )
        high = lax.ppermute(lax.slice_in_dim(block, 0, width, axis=dim), axis, backward)
        block = jnp.concatenate([low, block, high], axis=dim)
    return block


def side_by_side(parts):
    n, j, r, m = parts.shape
    return parts.transpose(0, 2, 1, 3).reshape(n, r, j * m)


def body(
    density,
    basis,
    near_list,
    near_blocks,
    far_leaf,
    leaf_coupling,
    transfer,
    far_coarse,
    coarse_coupling,
):
    leaf_count, rhs_count, leaf_width = density.shape
    rank_width = basis.shape[1]
    box_count = transfer.shape[0]
    child_count = leaf_count // box_count
    far_count = far_leaf.shape[1]
    coarse_count = far_coarse.shape[1]
    skeleton = jnp.einsum(
        "lrp,lkp->lrk", density, basis, preferred_element_type=jnp.float32
    ).astype(jnp.bfloat16)
    children = skeleton.reshape(box_count, child_count, rhs_count, rank_width)
    coarse = jnp.einsum(
        "ckq,crq->crk", transfer, side_by_side(children), preferred_element_type=jnp.float32
    ).astype(jnp.bfloat16)
    coarse_flat = coarse.reshape(box_count, rhs_count * rank_width)
    everything = coarse_flat
    for axes in STAGES:
        n = lax.axis_size(axes)
        spread = jnp.broadcast_to(everything[None], (n,) + everything.shape)
        everything = lax.all_to_all(spread, axes, 0, 0, tiled=False).reshape(
            (n * everything.shape[0],) + everything.shape[1:]
        )
    partner = lax.ppermute(everything, PAIR, [(0, 1), (1, 0)])
    everything = jnp.concatenate([everything, partner], axis=0)
    offset_base = lax.axis_index(ALL) * leaf_count - leaf_count
    density_flat = density.reshape(leaf_count, rhs_count * leaf_width)
    skeleton_flat = skeleton.reshape(leaf_count, rhs_count * rank_width)
    both_padded = with_halo(
        jnp.concatenate([density_flat, skeleton_flat], axis=1), ((ALL, 0),), leaf_count
    )
    density_padded = both_padded[:, : density_flat.shape[1]]
    skeleton_padded = both_padded[:, density_flat.shape[1] :]
    near_rows = jnp.take(density_padded, near_list - offset_base, axis=0).reshape(
        leaf_count, near_list.shape[1], rhs_count, leaf_width
    )
    near_part = jnp.einsum(
        "ljpq,ljrq->lrp", near_blocks, near_rows, preferred_element_type=jnp.float32
    )
    far_skels = jnp.take(skeleton_padded, far_leaf - offset_base, axis=0).reshape(
        leaf_count, far_count, rhs_count, rank_width
    )
    leaf_far = jnp.einsum(
        "lkq,lrq->lrk", leaf_coupling, side_by_side(far_skels), preferred_element_type=jnp.float32
    )
    near_part, leaf_far = lax.optimization_barrier((near_part, leaf_far))
    sizes = [lax.axis_size(a) for a in ALL]
    owner, slot = far_coarse // box_count, far_coarse % box_count
    coords = []
    for size in reversed(sizes):
        coords.append(owner % size)
        owner = owner // size
    coords = dict(zip(reversed(ALL), coords))
    position = (coords[PAIR] != lax.axis_index(PAIR)).astype(jnp.int32)
    for axes in reversed(STAGES):
        for a in axes:
            position = position * lax.axis_size(a) + coords[a]
    coarse_skels = jnp.take(everything, position * box_count + slot, axis=0).reshape(
        box_count, coarse_count, rhs_count, rank_width
    )
    coarse_field = jnp.einsum(
        "ckq,crq->crk", coarse_coupling, side_by_side(coarse_skels), preferred_element_type=jnp.float32
    ).astype(jnp.bfloat16)
    descended = jnp.einsum(
        "crk,ckq->crq", coarse_field, transfer, preferred_element_type=jnp.float32
    )
    descended = (
        descended.reshape(box_count, rhs_count, child_count, rank_width)
        .transpose(0, 2, 1, 3)
        .reshape(leaf_count, rhs_count, rank_width)
    )
    local_field = (leaf_far + descended).astype(jnp.bfloat16)
    total = (
        jnp.einsum("lrk,lkp->lrp", local_field, basis, preferred_element_type=jnp.float32)
        + near_part
    )
    return total.astype(jnp.bfloat16)


def solution(mesh):
    assert tuple(mesh.shape.values()) == (64, 4)
    grid = Mesh(mesh.devices.reshape(8, 4, 2, 2, 2), ALL)
    return jax.shard_map(
        body,
        mesh=grid,
        in_specs=(
            P(ALL, None, None),
            P(ALL, None, None),
            P(ALL, None),
            P(ALL, None, None, None),
            P(ALL, None),
            P(ALL, None, None),
            P(ALL, None, None),
            P(ALL, None),
            P(ALL, None, None),
        ),
        out_specs=P(ALL, None, None),
        check_vma=False,
    )
```

```python
import jax
import jax.numpy as jnp
from jax import lax
from jax.sharding import Mesh, PartitionSpec as P

ALL = ("z", "x", "y_lo", "y_hi", "core")
STAGES = (("z",), ("x", "y_lo", "y_hi"))
PAIR = "core"


def with_halo(block, sides, width):
    for axis, dim in sides:
        count = lax.axis_size(axis)
        forward = [(i, i + 1) for i in range(count - 1)]
        backward = [(target, source) for source, target in forward]
        low = lax.ppermute(
            lax.slice_in_dim(block, block.shape[dim] - width, None, axis=dim), axis, forward
        )
        high = lax.ppermute(lax.slice_in_dim(block, 0, width, axis=dim), axis, backward)
        block = jnp.concatenate([low, block, high], axis=dim)
    return block


def side_by_side(parts):
    n, j, r, m = parts.shape
    return parts.transpose(0, 2, 1, 3).reshape(n, r, j * m)


def body(
    density,
    basis,
    near_list,
    near_blocks,
    far_leaf,
    leaf_coupling,
    transfer,
    far_coarse,
    coarse_coupling,
):
    leaf_count, rhs_count, leaf_width = density.shape
    rank_width = basis.shape[1]
    box_count = transfer.shape[0]
    child_count = leaf_count // box_count
    far_count = far_leaf.shape[1]
    coarse_count = far_coarse.shape[1]
    skeleton = jnp.einsum(
        "lrp,lkp->lrk", density, basis, preferred_element_type=jnp.float32
    ).astype(jnp.bfloat16)
    children = skeleton.reshape(box_count, child_count, rhs_count, rank_width)
    coarse = jnp.einsum(
        "ckq,crq->crk", transfer, side_by_side(children), preferred_element_type=jnp.float32
    ).astype(jnp.bfloat16)
    coarse_flat = coarse.reshape(box_count, rhs_count * rank_width)
    everything = coarse_flat
    for axes in STAGES:
        n = lax.axis_size(axes)
        spread = jnp.broadcast_to(everything[None], (n,) + everything.shape)
        everything = lax.all_to_all(spread, axes, 0, 0, tiled=False).reshape(
            (n * everything.shape[0],) + everything.shape[1:]
        )
    offset_base = lax.axis_index(ALL) * leaf_count - leaf_count
    density_flat = density.reshape(leaf_count, rhs_count * leaf_width)
    skeleton_flat = skeleton.reshape(leaf_count, rhs_count * rank_width)
    both_padded = with_halo(
        jnp.concatenate([density_flat, skeleton_flat], axis=1), ((ALL, 0),), leaf_count
    )
    density_padded = both_padded[:, : density_flat.shape[1]]
    skeleton_padded = both_padded[:, density_flat.shape[1] :]
    near_rows = jnp.take(density_padded, near_list - offset_base, axis=0).reshape(
        leaf_count, near_list.shape[1], rhs_count, leaf_width
    )
    near_part = jnp.einsum(
        "ljpq,ljrq->lrp", near_blocks, near_rows, preferred_element_type=jnp.float32
    )
    far_skels = jnp.take(skeleton_padded, far_leaf - offset_base, axis=0).reshape(
        leaf_count, far_count, rhs_count, rank_width
    )
    leaf_far = jnp.einsum(
        "lkq,lrq->lrk", leaf_coupling, side_by_side(far_skels), preferred_element_type=jnp.float32
    )
    everything, near_part, leaf_far = lax.optimization_barrier((everything, near_part, leaf_far))
    partner = lax.ppermute(everything, PAIR, [(0, 1), (1, 0)])
    sizes = [lax.axis_size(a) for a in ALL]
    owner, slot = far_coarse // box_count, far_coarse % box_count
    coords = []
    for size in reversed(sizes):
        coords.append(owner % size)
        owner = owner // size
    coords = dict(zip(reversed(ALL), coords))
    position = 0
    for axes in reversed(STAGES):
        for a in axes:
            position = position * lax.axis_size(a) + coords[a]
    row = position * box_count + slot
    coarse_skels = jnp.where(
        (coords[PAIR] != lax.axis_index(PAIR))[:, :, None],
        jnp.take(partner, row, axis=0),
        jnp.take(everything, row, axis=0),
    ).reshape(box_count, coarse_count, rhs_count, rank_width)
    coarse_field = jnp.einsum(
        "ckq,crq->crk", coarse_coupling, side_by_side(coarse_skels), preferred_element_type=jnp.float32
    ).astype(jnp.bfloat16)
    descended = jnp.einsum(
        "crk,ckq->crq", coarse_field, transfer, preferred_element_type=jnp.float32
    )
    descended = (
        descended.reshape(box_count, rhs_count, child_count, rank_width)
        .transpose(0, 2, 1, 3)
        .reshape(leaf_count, rhs_count, rank_width)
    )
    local_field = (leaf_far + descended).astype(jnp.bfloat16)
    total = (
        jnp.einsum("lrk,lkp->lrp", local_field, basis, preferred_element_type=jnp.float32)
        + near_part
    )
    return total.astype(jnp.bfloat16)


def solution(mesh):
    assert tuple(mesh.shape.values()) == (64, 4)
    grid = Mesh(mesh.devices.reshape(8, 4, 2, 2, 2), ALL)
    return jax.shard_map(
        body,
        mesh=grid,
        in_specs=(
            P(ALL, None, None),
            P(ALL, None, None),
            P(ALL, None),
            P(ALL, None, None, None),
            P(ALL, None),
            P(ALL, None, None),
            P(ALL, None, None),
            P(ALL, None),
            P(ALL, None, None),
        ),
        out_specs=P(ALL, None, None),
        check_vma=False,
    )
```

```python
import jax
import jax.numpy as jnp
from jax import lax
from jax.sharding import Mesh, PartitionSpec as P

ALL = ("z", "x", "y_lo", "y_hi", "core")
STAGES = (("z",), ("x", "y_lo", "y_hi"))
PAIR = "core"


def side_by_side(parts):
    n, j, r, m = parts.shape
    return parts.transpose(0, 2, 1, 3).reshape(n, r, j * m)


def body(
    density,
    basis,
    near_list,
    near_blocks,
    far_leaf,
    leaf_coupling,
    transfer,
    far_coarse,
    coarse_coupling,
):
    leaf_count, rhs_count, leaf_width = density.shape
    rank_width = basis.shape[1]
    box_count = transfer.shape[0]
    child_count = leaf_count // box_count
    far_count = far_leaf.shape[1]
    coarse_count = far_coarse.shape[1]
    skeleton = jnp.einsum(
        "lrp,lkp->lrk", density, basis, preferred_element_type=jnp.float32
    ).astype(jnp.bfloat16)
    children = skeleton.reshape(box_count, child_count, rhs_count, rank_width)
    coarse = jnp.einsum(
        "ckq,crq->crk", transfer, side_by_side(children), preferred_element_type=jnp.float32
    ).astype(jnp.bfloat16)
    coarse_flat = coarse.reshape(box_count, rhs_count * rank_width)
    density_flat = density.reshape(leaf_count, rhs_count * leaf_width)
    skeleton_flat = skeleton.reshape(leaf_count, rhs_count * rank_width)
    device_count = lax.axis_size(ALL)
    me = lax.axis_index(ALL)
    even = lax.axis_index(PAIR) == 0
    own = jnp.concatenate([density_flat, skeleton_flat], axis=1)
    cross_pairs = [(d, d + 1) for d in range(1, device_count - 1, 2)]
    cross_pairs += [(d + 1, d) for d in range(1, device_count - 1, 2)]
    cross = lax.ppermute(own, ALL, cross_pairs)
    width = own.shape[1]
    coarse_rows = -(-coarse_flat.size // width)
    packed = jnp.pad(coarse_flat.reshape(1, -1), ((0, 0), (0, coarse_rows * width - coarse_flat.size)))
    received = lax.ppermute(
        jnp.concatenate([own, packed.reshape(coarse_rows, width)], axis=0), PAIR, [(0, 1), (1, 0)]
    )
    pair_halo = received[:leaf_count]
    pair_coarse = received[leaf_count:].reshape(-1)[: coarse_flat.size].reshape(coarse_flat.shape)
    padded = jnp.concatenate([pair_halo, own, cross], axis=0)
    density_padded = padded[:, : density_flat.shape[1]]
    skeleton_padded = padded[:, density_flat.shape[1] :]
    everything = jnp.concatenate([coarse_flat, pair_coarse], axis=0)
    for axes in STAGES:
        n = lax.axis_size(axes)
        spread = jnp.broadcast_to(everything[None], (n,) + everything.shape)
        everything = lax.all_to_all(spread, axes, 0, 0, tiled=False).reshape(
            (n * everything.shape[0],) + everything.shape[1:]
        )

    def halo_row(index):
        t = index - me * leaf_count
        low = jnp.where(even, t + 3 * leaf_count, t + leaf_count)
        high = jnp.where(even, t - leaf_count, t + leaf_count)
        return jnp.where(t < 0, low, jnp.where(t < leaf_count, t + leaf_count, high))
    near_rows = jnp.take(density_padded, halo_row(near_list), axis=0).reshape(
        leaf_count, near_list.shape[1], rhs_count, leaf_width
    )
    near_part = jnp.einsum(
        "ljpq,ljrq->lrp", near_blocks, near_rows, preferred_element_type=jnp.float32
    )
    far_skels = jnp.take(skeleton_padded, halo_row(far_leaf), axis=0).reshape(
        leaf_count, far_count, rhs_count, rank_width
    )
    leaf_far = jnp.einsum(
        "lkq,lrq->lrk", leaf_coupling, side_by_side(far_skels), preferred_element_type=jnp.float32
    )
    everything, near_part, leaf_far = lax.optimization_barrier((everything, near_part, leaf_far))

    sizes = [lax.axis_size(a) for a in ALL]
    owner, slot = far_coarse // box_count, far_coarse % box_count
    coords = []
    for size in reversed(sizes):
        coords.append(owner % size)
        owner = owner // size
    coords = dict(zip(reversed(ALL), coords))
    position = 0
    for axes in reversed(STAGES):
        for a in axes:
            position = position * lax.axis_size(a) + coords[a]
    position = position * 2 + (coords[PAIR] != lax.axis_index(PAIR)).astype(jnp.int32)
    coarse_skels = jnp.take(everything, position * box_count + slot, axis=0).reshape(
        box_count, coarse_count, rhs_count, rank_width
    )
    coarse_field = jnp.einsum(
        "ckq,crq->crk", coarse_coupling, side_by_side(coarse_skels), preferred_element_type=jnp.float32
    ).astype(jnp.bfloat16)
    descended = jnp.einsum(
        "crk,ckq->crq", coarse_field, transfer, preferred_element_type=jnp.float32
    )
    descended = (
        descended.reshape(box_count, rhs_count, child_count, rank_width)
        .transpose(0, 2, 1, 3)
        .reshape(leaf_count, rhs_count, rank_width)
    )
    local_field = (leaf_far + descended).astype(jnp.bfloat16)
    total = (
        jnp.einsum("lrk,lkp->lrp", local_field, basis, preferred_element_type=jnp.float32)
        + near_part
    )
    return total.astype(jnp.bfloat16)


def solution(mesh):
    assert tuple(mesh.shape.values()) == (64, 4)
    grid = Mesh(mesh.devices.reshape(8, 4, 2, 2, 2), ALL)
    return jax.shard_map(
        body,
        mesh=grid,
        in_specs=(
            P(ALL, None, None),
            P(ALL, None, None),
            P(ALL, None),
            P(ALL, None, None, None),
            P(ALL, None),
            P(ALL, None, None),
            P(ALL, None, None),
            P(ALL, None),
            P(ALL, None, None),
        ),
        out_specs=P(ALL, None, None),
        check_vma=False,
    )
```

```python
import jax
import jax.numpy as jnp
from jax import lax
from jax.sharding import Mesh, PartitionSpec as P


ALL = ("z", "x", "y_lo", "y_hi", "core")
STAGES = (("x", "y_lo", "y_hi"), ("z",))
PAIR = "core"


def with_halo(block, sides, width):
    for axis, dim in sides:
        count = lax.axis_size(axis)
        forward = [(i, i + 1) for i in range(count - 1)]
        backward = [(target, source) for source, target in forward]
        low = lax.ppermute(
            lax.slice_in_dim(block, block.shape[dim] - width, None, axis=dim), axis, forward
        )
        high = lax.ppermute(lax.slice_in_dim(block, 0, width, axis=dim), axis, backward)
        block = jnp.concatenate([low, block, high], axis=dim)
    return block


def side_by_side(parts):
    n, j, r, m = parts.shape
    return parts.transpose(0, 2, 1, 3).reshape(n, r, j * m)


def body(
    density,
    basis,
    near_list,
    near_blocks,
    far_leaf,
    leaf_coupling,
    transfer,
    far_coarse,
    coarse_coupling,
):
    leaf_count, rhs_count, leaf_width = density.shape
    rank_width = basis.shape[1]
    box_count = transfer.shape[0]
    child_count = leaf_count // box_count
    far_count = far_leaf.shape[1]
    coarse_count = far_coarse.shape[1]
    skeleton = jnp.einsum(
        "lrp,lkp->lrk", density, basis, preferred_element_type=jnp.float32
    ).astype(jnp.bfloat16)
    children = skeleton.reshape(box_count, child_count, rhs_count, rank_width)
    coarse = jnp.einsum(
        "ckq,crq->crk", transfer, side_by_side(children), preferred_element_type=jnp.float32
    ).astype(jnp.bfloat16)
    coarse_flat = coarse.reshape(box_count, rhs_count * rank_width)
    everything = coarse_flat
    for axes in STAGES:
        n = lax.axis_size(axes)
        spread = jnp.broadcast_to(everything[None], (n,) + everything.shape)
        moved = lax.all_to_all(spread, axes, 0, 0, tiled=False)
        everything = moved.reshape(
            (n * everything.shape[0],) + everything.shape[1:]
        )
    offset_base = lax.axis_index(ALL) * leaf_count - leaf_count
    partner_far = lax.ppermute(far_coarse, PAIR, [(0, 1), (1, 0)])
    density_flat = density.reshape(leaf_count, rhs_count * leaf_width)
    skeleton_flat = skeleton.reshape(leaf_count, rhs_count * rank_width)
    both_padded = with_halo(
        jnp.concatenate([density_flat, skeleton_flat], axis=1), ((ALL, 0),), leaf_count
    )
    density_padded = both_padded[:, : density_flat.shape[1]]
    skeleton_padded = both_padded[:, density_flat.shape[1] :]
    near_rows = jnp.take(density_padded, near_list - offset_base, axis=0).reshape(
        leaf_count, near_list.shape[1], rhs_count, leaf_width
    )
    near_part = jnp.einsum(
        "ljpq,ljrq->lrp", near_blocks, near_rows, preferred_element_type=jnp.float32
    )
    far_skels = jnp.take(skeleton_padded, far_leaf - offset_base, axis=0).reshape(
        leaf_count, far_count, rhs_count, rank_width
    )
    leaf_far = jnp.einsum(
        "lkq,lrq->lrk", leaf_coupling, side_by_side(far_skels), preferred_element_type=jnp.float32
    )
    everything, near_part, leaf_far = lax.optimization_barrier((everything, near_part, leaf_far))
    def placed(boxes):
        owner, slot = boxes // box_count, boxes % box_count
        coords = {}
        for a in reversed(ALL):
            coords[a] = owner % lax.axis_size(a)
            owner = owner // lax.axis_size(a)
        position = 0
        for axes in reversed(STAGES):
            for a in axes:
                position = position * lax.axis_size(a) + coords[a]
        return position * box_count + slot, coords[PAIR] != lax.axis_index(PAIR)

    row, elsewhere = placed(far_coarse)
    asked, _ = placed(partner_far)
    served = lax.ppermute(jnp.take(everything, asked, axis=0), PAIR, [(0, 1), (1, 0)])
    coarse_skels = jnp.where(
        elsewhere[:, :, None], served, jnp.take(everything, row, axis=0)
    ).reshape(box_count, coarse_count, rhs_count, rank_width)
    coarse_field = jnp.einsum(
        "ckq,crq->crk", coarse_coupling, side_by_side(coarse_skels), preferred_element_type=jnp.float32
    ).astype(jnp.bfloat16)
    descended = jnp.einsum(
        "crk,ckq->crq", coarse_field, transfer, preferred_element_type=jnp.float32
    )
    descended = (
        descended.reshape(box_count, rhs_count, child_count, rank_width)
        .transpose(0, 2, 1, 3)
        .reshape(leaf_count, rhs_count, rank_width)
    )
    local_field = (leaf_far + descended).astype(jnp.bfloat16)
    total = (
        jnp.einsum("lrk,lkp->lrp", local_field, basis, preferred_element_type=jnp.float32)
        + near_part
    )
    return total.astype(jnp.bfloat16)


def solution(mesh):
    assert tuple(mesh.shape.values()) == (64, 4)
    grid = Mesh(mesh.devices.reshape(8, 4, 2, 2, 2), ALL)
    return jax.shard_map(
        body,
        mesh=grid,
        in_specs=(
            P(ALL, None, None),
            P(ALL, None, None),
            P(ALL, None),
            P(ALL, None, None, None),
            P(ALL, None),
            P(ALL, None, None),
            P(ALL, None, None),
            P(ALL, None),
            P(ALL, None, None),
        ),
        out_specs=P(ALL, None, None),
        check_vma=False,
    )
```

```python
import jax
import jax.numpy as jnp
from jax import lax
from jax.sharding import Mesh, PartitionSpec as P


ALL = ("z", "x", "y_lo", "y_hi", "core")
STAGES = (("z",), ("x", "y_lo", "y_hi"))
PAIR = "core"


def side_by_side(parts):
    n, j, r, m = parts.shape
    return parts.transpose(0, 2, 1, 3).reshape(n, r, j * m)


def body(
    density,
    basis,
    near_list,
    near_blocks,
    far_leaf,
    leaf_coupling,
    transfer,
    far_coarse,
    coarse_coupling,
):
    leaf_count, rhs_count, leaf_width = density.shape
    rank_width = basis.shape[1]
    box_count = transfer.shape[0]
    child_count = leaf_count // box_count
    far_count = far_leaf.shape[1]
    coarse_count = far_coarse.shape[1]
    skeleton = jnp.einsum(
        "lrp,lkp->lrk", density, basis, preferred_element_type=jnp.float32
    ).astype(jnp.bfloat16)
    children = skeleton.reshape(box_count, child_count, rhs_count, rank_width)
    coarse = jnp.einsum(
        "ckq,crq->crk", transfer, side_by_side(children), preferred_element_type=jnp.float32
    ).astype(jnp.bfloat16)
    coarse_flat = coarse.reshape(box_count, rhs_count * rank_width)
    everything = coarse_flat
    for axes in STAGES:
        n = lax.axis_size(axes)
        spread = jnp.broadcast_to(everything[None], (n,) + everything.shape)
        moved = lax.all_to_all(spread, axes, 0, 0, tiled=False)
        everything = moved.reshape(
            (n * everything.shape[0],) + everything.shape[1:]
        )
    density_flat = density.reshape(leaf_count, rhs_count * leaf_width)
    skeleton_flat = skeleton.reshape(leaf_count, rhs_count * rank_width)
    device_count = lax.axis_size(ALL)
    me = lax.axis_index(ALL)
    even = lax.axis_index(PAIR) == 0
    own = jnp.concatenate([density_flat, skeleton_flat], axis=1)
    width = own.shape[1]
    digits = jnp.stack([far_coarse // 32, far_coarse % 32]).reshape(1, -1).astype(own.dtype)
    extra = jnp.pad(digits, ((0, 0), (0, width - digits.shape[1])))
    cross_pairs = [(d, d + 1) for d in range(1, device_count - 1, 2)]
    cross_pairs += [(d + 1, d) for d in range(1, device_count - 1, 2)]
    cross = lax.ppermute(own, ALL, cross_pairs)
    received = lax.ppermute(
        jnp.concatenate([own, extra], axis=0), PAIR, [(0, 1), (1, 0)]
    )
    pair_halo = received[:leaf_count]
    got = received[leaf_count, : digits.shape[1]].astype(jnp.int32).reshape(2, *far_coarse.shape)
    partner_far = got[0] * 32 + got[1]
    padded = jnp.concatenate([pair_halo, own, cross], axis=0)
    density_padded = padded[:, : density_flat.shape[1]]
    skeleton_padded = padded[:, density_flat.shape[1] :]

    def halo_row(index):
        t = index - me * leaf_count
        low = jnp.where(even, t + 3 * leaf_count, t + leaf_count)
        high = jnp.where(even, t - leaf_count, t + leaf_count)
        return jnp.where(t < 0, low, jnp.where(t < leaf_count, t + leaf_count, high))

    near_rows = jnp.take(density_padded, halo_row(near_list), axis=0).reshape(
        leaf_count, near_list.shape[1], rhs_count, leaf_width
    )
    near_part = jnp.einsum(
        "ljpq,ljrq->lrp", near_blocks, near_rows, preferred_element_type=jnp.float32
    )
    far_skels = jnp.take(skeleton_padded, halo_row(far_leaf), axis=0).reshape(
        leaf_count, far_count, rhs_count, rank_width
    )
    leaf_far = jnp.einsum(
        "lkq,lrq->lrk", leaf_coupling, side_by_side(far_skels), preferred_element_type=jnp.float32
    )
    everything, near_part, leaf_far = lax.optimization_barrier((everything, near_part, leaf_far))

    def placed(boxes):
        owner, slot = boxes // box_count, boxes % box_count
        coords = {}
        for a in reversed(ALL):
            coords[a] = owner % lax.axis_size(a)
            owner = owner // lax.axis_size(a)
        position = 0
        for axes in reversed(STAGES):
            for a in axes:
                position = position * lax.axis_size(a) + coords[a]
        return position * box_count + slot, coords[PAIR] != lax.axis_index(PAIR)

    row, elsewhere = placed(far_coarse)
    asked, _ = placed(partner_far)
    served = lax.ppermute(jnp.take(everything, asked, axis=0), PAIR, [(0, 1), (1, 0)])
    coarse_skels = jnp.where(
        elsewhere[:, :, None], served, jnp.take(everything, row, axis=0)
    ).reshape(box_count, coarse_count, rhs_count, rank_width)
    coarse_field = jnp.einsum(
        "ckq,crq->crk", coarse_coupling, side_by_side(coarse_skels), preferred_element_type=jnp.float32
    ).astype(jnp.bfloat16)
    descended = jnp.einsum(
        "crk,ckq->crq", coarse_field, transfer, preferred_element_type=jnp.float32
    )
    descended = (
        descended.reshape(box_count, rhs_count, child_count, rank_width)
        .transpose(0, 2, 1, 3)
        .reshape(leaf_count, rhs_count, rank_width)
    )
    local_field = (leaf_far + descended).astype(jnp.bfloat16)
    total = (
        jnp.einsum("lrk,lkp->lrp", local_field, basis, preferred_element_type=jnp.float32)
        + near_part
    )
    return total.astype(jnp.bfloat16)


def solution(mesh):
    assert tuple(mesh.shape.values()) == (64, 4)
    grid = Mesh(mesh.devices.reshape(8, 4, 2, 2, 2), ALL)
    return jax.shard_map(
        body,
        mesh=grid,
        in_specs=(
            P(ALL, None, None),
            P(ALL, None, None),
            P(ALL, None),
            P(ALL, None, None, None),
            P(ALL, None),
            P(ALL, None, None),
            P(ALL, None, None),
            P(ALL, None),
            P(ALL, None, None),
        ),
        out_specs=P(ALL, None, None),
        check_vma=False,
    )
```

```python
import jax
import jax.numpy as jnp
from jax import lax
from jax.sharding import Mesh, PartitionSpec as P


ALL = ("z", "x", "y_lo", "y_hi", "core")
STAGES = (("z",), ("x", "y_lo", "y_hi"))
PAIR = "core"


def side_by_side(parts):
    n, j, r, m = parts.shape
    return parts.transpose(0, 2, 1, 3).reshape(n, r, j * m)


def body(
    density,
    basis,
    near_list,
    near_blocks,
    far_leaf,
    leaf_coupling,
    transfer,
    far_coarse,
    coarse_coupling,
):
    leaf_count, rhs_count, leaf_width = density.shape
    rank_width = basis.shape[1]
    box_count = transfer.shape[0]
    child_count = leaf_count // box_count
    far_count = far_leaf.shape[1]
    coarse_count = far_coarse.shape[1]
    skeleton = jnp.einsum(
        "lrp,lkp->lrk", density, basis, preferred_element_type=jnp.float32
    ).astype(jnp.bfloat16)
    children = skeleton.reshape(box_count, child_count, rhs_count, rank_width)
    coarse = jnp.einsum(
        "ckq,crq->crk", transfer, side_by_side(children), preferred_element_type=jnp.float32
    ).astype(jnp.bfloat16)
    coarse_flat = coarse.reshape(box_count, rhs_count * rank_width)
    everything = coarse_flat
    for axes in STAGES:
        n = lax.axis_size(axes)
        spread = jnp.broadcast_to(everything[None], (n,) + everything.shape)
        moved = lax.all_to_all(spread, axes, 0, 0, tiled=False)
        everything = moved.reshape(
            (n * everything.shape[0],) + everything.shape[1:]
        )
    density_flat = density.reshape(leaf_count, rhs_count * leaf_width)
    skeleton_flat = skeleton.reshape(leaf_count, rhs_count * rank_width)
    device_count = lax.axis_size(ALL)
    me = lax.axis_index(ALL)
    even = lax.axis_index(PAIR) == 0
    own = jnp.concatenate([density_flat, skeleton_flat], axis=1)
    width = own.shape[1]
    digits = jnp.stack([far_coarse // 32, far_coarse % 32]).reshape(1, -1).astype(own.dtype)
    extra = jnp.pad(digits, ((0, 0), (0, width - digits.shape[1])))
    cross_pairs = [(d, d + 1) for d in range(1, device_count - 1, 2)]
    cross_pairs += [(d + 1, d) for d in range(1, device_count - 1, 2)]
    cross = lax.ppermute(own, ALL, cross_pairs)
    received = lax.ppermute(
        jnp.concatenate([own, extra], axis=0), PAIR, [(0, 1), (1, 0)]
    )
    pair_halo = received[:leaf_count]
    got = received[leaf_count, : digits.shape[1]].astype(jnp.int32).reshape(2, *far_coarse.shape)
    partner_far = got[0] * 32 + got[1]
    padded = jnp.concatenate([pair_halo, own, cross], axis=0)
    density_padded = padded[:, : density_flat.shape[1]]
    skeleton_padded = padded[:, density_flat.shape[1] :]

    def halo_row(index):
        t = index - me * leaf_count
        low = jnp.where(even, t + 3 * leaf_count, t + leaf_count)
        high = jnp.where(even, t - leaf_count, t + leaf_count)
        return jnp.where(t < 0, low, jnp.where(t < leaf_count, t + leaf_count, high))

    near_rows = jnp.take(density_padded, halo_row(near_list), axis=0, mode="clip").reshape(
        leaf_count, near_list.shape[1], rhs_count, leaf_width
    )
    near_part = jnp.einsum(
        "ljpq,ljrq->lrp", near_blocks, near_rows, preferred_element_type=jnp.float32
    )
    far_skels = jnp.take(skeleton_padded, halo_row(far_leaf), axis=0, mode="clip").reshape(
        leaf_count, far_count, rhs_count, rank_width
    )
    leaf_far = jnp.einsum(
        "lkq,lrq->lrk", leaf_coupling, side_by_side(far_skels), preferred_element_type=jnp.float32
    )
    everything, near_part, leaf_far = lax.optimization_barrier((everything, near_part, leaf_far))

    def placed(boxes):
        owner, slot = boxes // box_count, boxes % box_count
        coords = {}
        for a in reversed(ALL):
            coords[a] = owner % lax.axis_size(a)
            owner = owner // lax.axis_size(a)
        position = 0
        for axes in reversed(STAGES):
            for a in axes:
                position = position * lax.axis_size(a) + coords[a]
        return position * box_count + slot, coords[PAIR] != lax.axis_index(PAIR)

    row, elsewhere = placed(far_coarse)
    asked, _ = placed(partner_far)
    served = lax.ppermute(jnp.take(everything, asked, axis=0, mode="clip"), PAIR, [(0, 1), (1, 0)])
    coarse_skels = jnp.where(
        elsewhere[:, :, None], served, jnp.take(everything, row, axis=0, mode="clip")
    ).reshape(box_count, coarse_count, rhs_count, rank_width)
    coarse_field = jnp.einsum(
        "ckq,crq->crk", coarse_coupling, side_by_side(coarse_skels), preferred_element_type=jnp.float32
    ).astype(jnp.bfloat16)
    descended = jnp.einsum(
        "crk,ckq->crq", coarse_field, transfer, preferred_element_type=jnp.float32
    )
    descended = (
        descended.reshape(box_count, rhs_count, child_count, rank_width)
        .transpose(0, 2, 1, 3)
        .reshape(leaf_count, rhs_count, rank_width)
    )
    local_field = (leaf_far + descended).astype(jnp.bfloat16)
    total = (
        jnp.einsum("lrk,lkp->lrp", local_field, basis, preferred_element_type=jnp.float32)
        + near_part
    )
    return total.astype(jnp.bfloat16)


def solution(mesh):
    assert tuple(mesh.shape.values()) == (64, 4)
    grid = Mesh(mesh.devices.reshape(8, 4, 2, 2, 2), ALL)
    return jax.shard_map(
        body,
        mesh=grid,
        in_specs=(
            P(ALL, None, None),
            P(ALL, None, None),
            P(ALL, None),
            P(ALL, None, None, None),
            P(ALL, None),
            P(ALL, None, None),
            P(ALL, None, None),
            P(ALL, None),
            P(ALL, None, None),
        ),
        out_specs=P(ALL, None, None),
        check_vma=False,
    )
```

```python
import jax
import jax.numpy as jnp
from jax import lax
from jax.sharding import Mesh, PartitionSpec as P


ALL = ("z", "x", "y_lo", "y_hi", "core")
STAGES = (("z",), ("x", "y_lo", "y_hi"))
PAIR = "core"


def side_by_side(parts):
    n, j, r, m = parts.shape
    return parts.transpose(0, 2, 1, 3).reshape(n, r, j * m)


def body(
    density,
    basis,
    near_list,
    near_blocks,
    far_leaf,
    leaf_coupling,
    transfer,
    far_coarse,
    coarse_coupling,
):
    leaf_count, rhs_count, leaf_width = density.shape
    rank_width = basis.shape[1]
    box_count = transfer.shape[0]
    child_count = leaf_count // box_count
    far_count = far_leaf.shape[1]
    coarse_count = far_coarse.shape[1]
    skeleton = jnp.einsum(
        "lrp,lkp->lrk", density, basis, preferred_element_type=jnp.float32
    ).astype(jnp.bfloat16)
    children = skeleton.reshape(box_count, child_count, rhs_count, rank_width)
    coarse = jnp.einsum(
        "ckq,crq->crk", transfer, side_by_side(children), preferred_element_type=jnp.float32
    ).astype(jnp.bfloat16)
    coarse_flat = coarse.reshape(box_count, rhs_count * rank_width)
    everything = coarse_flat
    for axes in STAGES:
        n = lax.axis_size(axes)
        if len(axes) == 1:
            everything = lax.all_gather(everything, axes, axis=0, tiled=True)
        else:
            spread = jnp.broadcast_to(everything[None], (n,) + everything.shape)
            moved = lax.all_to_all(spread, axes, 0, 0, tiled=False)
            everything = moved.reshape((n * everything.shape[0],) + everything.shape[1:])
    density_flat = density.reshape(leaf_count, rhs_count * leaf_width)
    skeleton_flat = skeleton.reshape(leaf_count, rhs_count * rank_width)
    device_count = lax.axis_size(ALL)
    me = lax.axis_index(ALL)
    even = lax.axis_index(PAIR) == 0
    own = jnp.concatenate([density_flat, skeleton_flat], axis=1)
    width = own.shape[1]
    digits = jnp.stack([far_coarse // 32, far_coarse % 32]).reshape(1, -1).astype(own.dtype)
    extra = jnp.pad(digits, ((0, 0), (0, width - digits.shape[1])))
    cross_pairs = [(d, d + 1) for d in range(1, device_count - 1, 2)]
    cross_pairs += [(d + 1, d) for d in range(1, device_count - 1, 2)]
    cross = lax.ppermute(own, ALL, cross_pairs)
    received = lax.ppermute(
        jnp.concatenate([own, extra], axis=0), PAIR, [(0, 1), (1, 0)]
    )
    pair_halo = received[:leaf_count]
    got = received[leaf_count, : digits.shape[1]].astype(jnp.int32).reshape(2, *far_coarse.shape)
    partner_far = got[0] * 32 + got[1]
    padded = jnp.concatenate([pair_halo, own, cross], axis=0)
    density_padded = padded[:, : density_flat.shape[1]]
    skeleton_padded = padded[:, density_flat.shape[1] :]

    def halo_row(index):
        t = index - me * leaf_count
        low = jnp.where(even, t + 3 * leaf_count, t + leaf_count)
        high = jnp.where(even, t - leaf_count, t + leaf_count)
        return jnp.where(t < 0, low, jnp.where(t < leaf_count, t + leaf_count, high))

    near_rows = jnp.take(density_padded, halo_row(near_list), axis=0, mode="clip").reshape(
        leaf_count, near_list.shape[1], rhs_count, leaf_width
    )
    near_part = jnp.einsum(
        "ljpq,ljrq->lrp", near_blocks, near_rows, preferred_element_type=jnp.float32
    )
    far_skels = jnp.take(skeleton_padded, halo_row(far_leaf), axis=0, mode="clip").reshape(
        leaf_count, far_count, rhs_count, rank_width
    )
    leaf_far = jnp.einsum(
        "lkq,lrq->lrk", leaf_coupling, side_by_side(far_skels), preferred_element_type=jnp.float32
    )
    everything, near_part, leaf_far = lax.optimization_barrier((everything, near_part, leaf_far))

    def placed(boxes):
        owner, slot = boxes // box_count, boxes % box_count
        coords = {}
        for a in reversed(ALL):
            coords[a] = owner % lax.axis_size(a)
            owner = owner // lax.axis_size(a)
        position = 0
        for axes in reversed(STAGES):
            for a in axes:
                position = position * lax.axis_size(a) + coords[a]
        return position * box_count + slot, coords[PAIR] != lax.axis_index(PAIR)

    row, elsewhere = placed(far_coarse)
    asked, _ = placed(partner_far)
    served = lax.ppermute(jnp.take(everything, asked, axis=0, mode="clip"), PAIR, [(0, 1), (1, 0)])
    coarse_skels = jnp.where(
        elsewhere[:, :, None], served, jnp.take(everything, row, axis=0, mode="clip")
    ).reshape(box_count, coarse_count, rhs_count, rank_width)
    coarse_field = jnp.einsum(
        "ckq,crq->crk", coarse_coupling, side_by_side(coarse_skels), preferred_element_type=jnp.float32
    ).astype(jnp.bfloat16)
    descended = jnp.einsum(
        "crk,ckq->crq", coarse_field, transfer, preferred_element_type=jnp.float32
    )
    descended = (
        descended.reshape(box_count, rhs_count, child_count, rank_width)
        .transpose(0, 2, 1, 3)
        .reshape(leaf_count, rhs_count, rank_width)
    )
    local_field = (leaf_far + descended).astype(jnp.bfloat16)
    total = (
        jnp.einsum("lrk,lkp->lrp", local_field, basis, preferred_element_type=jnp.float32)
        + near_part
    )
    return total.astype(jnp.bfloat16)


def solution(mesh):
    assert tuple(mesh.shape.values()) == (64, 4)
    grid = Mesh(mesh.devices.reshape(8, 4, 2, 2, 2), ALL)
    return jax.shard_map(
        body,
        mesh=grid,
        in_specs=(
            P(ALL, None, None),
            P(ALL, None, None),
            P(ALL, None),
            P(ALL, None, None, None),
            P(ALL, None),
            P(ALL, None, None),
            P(ALL, None, None),
            P(ALL, None),
            P(ALL, None, None),
        ),
        out_specs=P(ALL, None, None),
        check_vma=False,
    )
```

```python
import jax
import jax.numpy as jnp
from jax import lax
from jax.sharding import Mesh, PartitionSpec as P


ALL = ("z", "x", "y_lo", "y_hi", "core")
STAGES = (("z",), ("x", "y_lo", "y_hi"))
PAIR = "core"


def side_by_side(parts):
    n, j, r, m = parts.shape
    return parts.transpose(0, 2, 1, 3).reshape(n, r, j * m)


def body(
    density,
    basis,
    near_list,
    near_blocks,
    far_leaf,
    leaf_coupling,
    transfer,
    far_coarse,
    coarse_coupling,
):
    leaf_count, rhs_count, leaf_width = density.shape
    rank_width = basis.shape[1]
    box_count = transfer.shape[0]
    child_count = leaf_count // box_count
    far_count = far_leaf.shape[1]
    coarse_count = far_coarse.shape[1]
    skeleton = jnp.einsum(
        "lrp,lkp->lrk", density, basis, preferred_element_type=jnp.float32
    ).astype(jnp.bfloat16)
    children = skeleton.reshape(box_count, child_count, rhs_count, rank_width)
    coarse = jnp.einsum(
        "ckq,crq->crk", transfer, side_by_side(children), preferred_element_type=jnp.float32
    ).astype(jnp.bfloat16)
    coarse_flat = coarse.reshape(box_count, rhs_count * rank_width)
    everything = coarse_flat
    for axes in STAGES:
        n = lax.axis_size(axes)
        spread = jnp.broadcast_to(everything[None], (n,) + everything.shape)
        moved = lax.all_to_all(spread, axes, 0, 0, tiled=False)
        everything = moved.reshape(
            (n * everything.shape[0],) + everything.shape[1:]
        )
    density_flat = density.reshape(leaf_count, rhs_count * leaf_width)
    skeleton_flat = skeleton.reshape(leaf_count, rhs_count * rank_width)
    device_count = lax.axis_size(ALL)
    me = lax.axis_index(ALL)
    even = lax.axis_index(PAIR) == 0
    own = jnp.concatenate([density_flat, skeleton_flat], axis=1)
    width = own.shape[1]
    digits = jnp.stack([far_coarse // 32, far_coarse % 32]).reshape(1, -1).astype(own.dtype)
    extra = jnp.pad(digits, ((0, 0), (0, width - digits.shape[1])))
    cross_pairs = [(d, d + 1) for d in range(1, device_count - 1, 2)]
    cross_pairs += [(d + 1, d) for d in range(1, device_count - 1, 2)]
    cross = lax.ppermute(own, ALL, cross_pairs)
    received = lax.ppermute(
        jnp.concatenate([own, extra], axis=0), PAIR, [(0, 1), (1, 0)]
    )
    pair_halo = received[:leaf_count]
    got = received[leaf_count, : digits.shape[1]].astype(jnp.int32).reshape(2, *far_coarse.shape)
    partner_far = got[0] * 32 + got[1]
    padded = jnp.concatenate([pair_halo, own, cross], axis=0)
    density_padded = padded[:, : density_flat.shape[1]]
    skeleton_padded = padded[:, density_flat.shape[1] :]

    def halo_row(index):
        t = index - me * leaf_count
        low = jnp.where(even, t + 3 * leaf_count, t + leaf_count)
        high = jnp.where(even, t - leaf_count, t + leaf_count)
        return jnp.where(t < 0, low, jnp.where(t < leaf_count, t + leaf_count, high))

    near_rows = jnp.take(density_padded, halo_row(near_list), axis=0, mode="clip").reshape(
        leaf_count, near_list.shape[1], rhs_count, leaf_width
    )
    half = leaf_count // 2
    near_early = jnp.einsum(
        "ljpq,ljrq->lrp", near_blocks[:half], near_rows[:half], preferred_element_type=jnp.float32
    )
    near_late = jnp.einsum(
        "ljpq,ljrq->lrp", near_blocks[half:], near_rows[half:], preferred_element_type=jnp.float32
    )
    far_skels = jnp.take(skeleton_padded, halo_row(far_leaf), axis=0, mode="clip").reshape(
        leaf_count, far_count, rhs_count, rank_width
    )
    leaf_far = jnp.einsum(
        "lkq,lrq->lrk", leaf_coupling, side_by_side(far_skels), preferred_element_type=jnp.float32
    )
    everything, near_early, leaf_far = lax.optimization_barrier((everything, near_early, leaf_far))
    near_late = lax.optimization_barrier(near_late)
    near_part = jnp.concatenate([near_early, near_late], axis=0)

    def placed(boxes):
        owner, slot = boxes // box_count, boxes % box_count
        coords = {}
        for a in reversed(ALL):
            coords[a] = owner % lax.axis_size(a)
            owner = owner // lax.axis_size(a)
        position = 0
        for axes in reversed(STAGES):
            for a in axes:
                position = position * lax.axis_size(a) + coords[a]
        return position * box_count + slot, coords[PAIR] != lax.axis_index(PAIR)

    row, elsewhere = placed(far_coarse)
    asked, _ = placed(partner_far)
    served = lax.ppermute(jnp.take(everything, asked, axis=0, mode="clip"), PAIR, [(0, 1), (1, 0)])
    coarse_skels = jnp.where(
        elsewhere[:, :, None], served, jnp.take(everything, row, axis=0, mode="clip")
    ).reshape(box_count, coarse_count, rhs_count, rank_width)
    coarse_field = jnp.einsum(
        "ckq,crq->crk", coarse_coupling, side_by_side(coarse_skels), preferred_element_type=jnp.float32
    ).astype(jnp.bfloat16)
    descended = jnp.einsum(
        "crk,ckq->crq", coarse_field, transfer, preferred_element_type=jnp.float32
    )
    descended = (
        descended.reshape(box_count, rhs_count, child_count, rank_width)
        .transpose(0, 2, 1, 3)
        .reshape(leaf_count, rhs_count, rank_width)
    )
    local_field = (leaf_far + descended).astype(jnp.bfloat16)
    total = (
        jnp.einsum("lrk,lkp->lrp", local_field, basis, preferred_element_type=jnp.float32)
        + near_part
    )
    return total.astype(jnp.bfloat16)


def solution(mesh):
    assert tuple(mesh.shape.values()) == (64, 4)
    grid = Mesh(mesh.devices.reshape(8, 4, 2, 2, 2), ALL)
    return jax.shard_map(
        body,
        mesh=grid,
        in_specs=(
            P(ALL, None, None),
            P(ALL, None, None),
            P(ALL, None),
            P(ALL, None, None, None),
            P(ALL, None),
            P(ALL, None, None),
            P(ALL, None, None),
            P(ALL, None),
            P(ALL, None, None),
        ),
        out_specs=P(ALL, None, None),
        check_vma=False,
    )
```

```python
import jax
import jax.numpy as jnp
from jax import lax
from jax.sharding import Mesh, PartitionSpec as P


ALL = ("z", "x", "y_lo", "y_hi", "core")
STAGES = (("z",), ("x", "y_lo", "y_hi"))
PAIR = "core"


def side_by_side(parts):
    n, j, r, m = parts.shape
    return parts.transpose(0, 2, 1, 3).reshape(n, r, j * m)


def body(
    density,
    basis,
    near_list,
    near_blocks,
    far_leaf,
    leaf_coupling,
    transfer,
    far_coarse,
    coarse_coupling,
):
    leaf_count, rhs_count, leaf_width = density.shape
    rank_width = basis.shape[1]
    box_count = transfer.shape[0]
    child_count = leaf_count // box_count
    far_count = far_leaf.shape[1]
    coarse_count = far_coarse.shape[1]
    skeleton = jnp.einsum(
        "lrp,lkp->lrk", density, basis, preferred_element_type=jnp.float32
    ).astype(jnp.bfloat16)
    children = skeleton.reshape(box_count, child_count, rhs_count, rank_width)
    coarse = jnp.einsum(
        "ckq,crq->crk", transfer, side_by_side(children), preferred_element_type=jnp.float32
    ).astype(jnp.bfloat16)
    coarse_flat = coarse.reshape(box_count, rhs_count * rank_width)
    everything = coarse_flat
    for axes in STAGES:
        n = lax.axis_size(axes)
        spread = jnp.broadcast_to(everything[None], (n,) + everything.shape)
        moved = lax.all_to_all(spread, axes, 0, 0, tiled=False)
        everything = moved.reshape(
            (n * everything.shape[0],) + everything.shape[1:]
        )
    density_flat = density.reshape(leaf_count, rhs_count * leaf_width)
    skeleton_flat = skeleton.reshape(leaf_count, rhs_count * rank_width)
    device_count = lax.axis_size(ALL)
    me = lax.axis_index(ALL)
    even = lax.axis_index(PAIR) == 0
    own = jnp.concatenate([density_flat, skeleton_flat], axis=1)
    width = own.shape[1]
    digits = jnp.stack([far_coarse // 32, far_coarse % 32]).reshape(1, -1).astype(own.dtype)
    extra = jnp.pad(digits, ((0, 0), (0, width - digits.shape[1])))
    cross_pairs = [(d, d + 1) for d in range(1, device_count - 1, 2)]
    cross_pairs += [(d + 1, d) for d in range(1, device_count - 1, 2)]
    cross = lax.ppermute(own, ALL, cross_pairs)
    received = lax.ppermute(
        jnp.concatenate([own, extra], axis=0), PAIR, [(0, 1), (1, 0)]
    )
    pair_halo = received[:leaf_count]
    got = received[leaf_count, : digits.shape[1]].astype(jnp.int32).reshape(2, *far_coarse.shape)
    partner_far = got[0] * 32 + got[1]
    padded = jnp.concatenate([pair_halo, own, cross], axis=0)
    density_padded = padded[:, : density_flat.shape[1]]
    skeleton_padded = padded[:, density_flat.shape[1] :]

    def halo_row(index):
        t = index - me * leaf_count
        low = jnp.where(even, t + 3 * leaf_count, t + leaf_count)
        high = jnp.where(even, t - leaf_count, t + leaf_count)
        return jnp.where(t < 0, low, jnp.where(t < leaf_count, t + leaf_count, high))

    near_index, far_index = halo_row(near_list), halo_row(far_leaf)

    near_rows = jnp.take(density_padded, near_index, axis=0).reshape(
        leaf_count, near_list.shape[1], rhs_count, leaf_width
    )
    near_part = jnp.einsum(
        "ljpq,ljrq->lrp", near_blocks, near_rows, preferred_element_type=jnp.float32
    )
    far_skels = jnp.take(skeleton_padded, far_index, axis=0).reshape(
        leaf_count, far_count, rhs_count, rank_width
    )
    leaf_far = jnp.einsum(
        "lkq,lrq->lrk", leaf_coupling, side_by_side(far_skels), preferred_element_type=jnp.float32
    )
    everything, near_part, leaf_far = lax.optimization_barrier((everything, near_part, leaf_far))

    def placed(boxes):
        owner, slot = boxes // box_count, boxes % box_count
        coords = {}
        for a in reversed(ALL):
            coords[a] = owner % lax.axis_size(a)
            owner = owner // lax.axis_size(a)
        position = 0
        for axes in reversed(STAGES):
            for a in axes:
                position = position * lax.axis_size(a) + coords[a]
        return position * box_count + slot, coords[PAIR] != lax.axis_index(PAIR)

    row, elsewhere = placed(far_coarse)
    asked, _ = placed(partner_far)
    served = lax.ppermute(jnp.take(everything, asked, axis=0), PAIR, [(0, 1), (1, 0)])
    coarse_skels = jnp.where(
        elsewhere[:, :, None], served, jnp.take(everything, row, axis=0)
    ).reshape(box_count, coarse_count, rhs_count, rank_width)
    coarse_field = jnp.einsum(
        "ckq,crq->crk", coarse_coupling, side_by_side(coarse_skels), preferred_element_type=jnp.float32
    ).astype(jnp.bfloat16)
    descended = jnp.einsum(
        "crk,ckq->crq", coarse_field, transfer, preferred_element_type=jnp.float32
    )
    descended = (
        descended.reshape(box_count, rhs_count, child_count, rank_width)
        .transpose(0, 2, 1, 3)
        .reshape(leaf_count, rhs_count, rank_width)
    )
    local_field = (leaf_far + descended).astype(jnp.bfloat16)
    total = (
        jnp.einsum("lrk,lkp->lrp", local_field, basis, preferred_element_type=jnp.float32)
        + near_part
    )
    return total.astype(jnp.bfloat16)


def solution(mesh):
    assert tuple(mesh.shape.values()) == (64, 4)
    grid = Mesh(mesh.devices.reshape(8, 4, 2, 2, 2), ALL)
    return jax.shard_map(
        body,
        mesh=grid,
        in_specs=(
            P(ALL, None, None),
            P(ALL, None, None),
            P(ALL, None),
            P(ALL, None, None, None),
            P(ALL, None),
            P(ALL, None, None),
            P(ALL, None, None),
            P(ALL, None),
            P(ALL, None, None),
        ),
        out_specs=P(ALL, None, None),
        check_vma=False,
    )
```

```python
import jax
import jax.numpy as jnp
from jax import lax
from jax.sharding import Mesh, PartitionSpec as P


ALL = ("z", "x", "y_lo", "y_hi", "core")
STAGES = (("z",), ("x", "y_lo", "y_hi"))
PAIR = "core"


def side_by_side(parts):
    n, j, r, m = parts.shape
    return parts.transpose(0, 2, 1, 3).reshape(n, r, j * m)


def body(
    density,
    basis,
    near_list,
    near_blocks,
    far_leaf,
    leaf_coupling,
    transfer,
    far_coarse,
    coarse_coupling,
):
    leaf_count, rhs_count, leaf_width = density.shape
    rank_width = basis.shape[1]
    box_count = transfer.shape[0]
    child_count = leaf_count // box_count
    far_count = far_leaf.shape[1]
    coarse_count = far_coarse.shape[1]
    skeleton = jnp.einsum(
        "lrp,lkp->lrk", density, basis, preferred_element_type=jnp.float32
    ).astype(jnp.bfloat16)
    children = skeleton.reshape(box_count, child_count, rhs_count, rank_width)
    coarse = jnp.einsum(
        "ckq,crq->crk", transfer, side_by_side(children), preferred_element_type=jnp.float32
    ).astype(jnp.bfloat16)
    coarse_flat = coarse.reshape(box_count, rhs_count * rank_width)
    everything = coarse_flat
    for axes in STAGES:
        n = lax.axis_size(axes)
        spread = jnp.broadcast_to(everything[None], (n,) + everything.shape)
        moved = lax.all_to_all(spread, axes, 0, 0, tiled=False)
        everything = moved.reshape(
            (n * everything.shape[0],) + everything.shape[1:]
        )
    density_flat = density.reshape(leaf_count, rhs_count * leaf_width)
    skeleton_flat = skeleton.reshape(leaf_count, rhs_count * rank_width)
    device_count = lax.axis_size(ALL)
    me = lax.axis_index(ALL)
    even = lax.axis_index(PAIR) == 0
    own = jnp.concatenate([density_flat, skeleton_flat], axis=1)
    width = own.shape[1]
    digits = jnp.stack([far_coarse // 32, far_coarse % 32]).reshape(1, -1).astype(own.dtype)
    extra = jnp.pad(digits, ((0, 0), (0, width - digits.shape[1])))
    cross_pairs = [(d, d + 1) for d in range(1, device_count - 1, 2)]
    cross_pairs += [(d + 1, d) for d in range(1, device_count - 1, 2)]
    cross = lax.ppermute(own, ALL, cross_pairs)
    received = lax.ppermute(
        jnp.concatenate([own, extra], axis=0), PAIR, [(0, 1), (1, 0)]
    )
    pair_halo = received[:leaf_count]
    got = received[leaf_count, : digits.shape[1]].astype(jnp.int32).reshape(2, *far_coarse.shape)
    partner_far = got[0] * 32 + got[1]
    padded = jnp.concatenate([pair_halo, own, cross], axis=0)
    density_padded = padded[:, : density_flat.shape[1]]
    skeleton_padded = padded[:, density_flat.shape[1] :]

    def halo_row(index):
        t = index - me * leaf_count
        low = jnp.where(even, t + 3 * leaf_count, t + leaf_count)
        high = jnp.where(even, t - leaf_count, t + leaf_count)
        return jnp.where(t < 0, low, jnp.where(t < leaf_count, t + leaf_count, high))

    near_rows = jnp.take(
        density_padded.reshape(-1, rhs_count, leaf_width), halo_row(near_list).reshape(-1), axis=0
    ).reshape(leaf_count, near_list.shape[1], rhs_count, leaf_width)
    near_part = jnp.einsum(
        "ljpq,ljrq->lrp", near_blocks, near_rows, preferred_element_type=jnp.float32
    )
    far_skels = jnp.take(skeleton_padded, halo_row(far_leaf), axis=0).reshape(
        leaf_count, far_count, rhs_count, rank_width
    )
    leaf_far = jnp.einsum(
        "lkq,lrq->lrk", leaf_coupling, side_by_side(far_skels), preferred_element_type=jnp.float32
    )
    everything, near_part, leaf_far = lax.optimization_barrier((everything, near_part, leaf_far))

    def placed(boxes):
        owner, slot = boxes // box_count, boxes % box_count
        coords = {}
        for a in reversed(ALL):
            coords[a] = owner % lax.axis_size(a)
            owner = owner // lax.axis_size(a)
        position = 0
        for axes in reversed(STAGES):
            for a in axes:
                position = position * lax.axis_size(a) + coords[a]
        return position * box_count + slot, coords[PAIR] != lax.axis_index(PAIR)

    row, elsewhere = placed(far_coarse)
    asked, _ = placed(partner_far)
    served = lax.ppermute(jnp.take(everything, asked, axis=0), PAIR, [(0, 1), (1, 0)])
    coarse_skels = jnp.where(
        elsewhere[:, :, None], served, jnp.take(everything, row, axis=0)
    ).reshape(box_count, coarse_count, rhs_count, rank_width)
    coarse_field = jnp.einsum(
        "ckq,crq->crk", coarse_coupling, side_by_side(coarse_skels), preferred_element_type=jnp.float32
    ).astype(jnp.bfloat16)
    descended = jnp.einsum(
        "crk,ckq->crq", coarse_field, transfer, preferred_element_type=jnp.float32
    )
    descended = (
        descended.reshape(box_count, rhs_count, child_count, rank_width)
        .transpose(0, 2, 1, 3)
        .reshape(leaf_count, rhs_count, rank_width)
    )
    local_field = (leaf_far + descended).astype(jnp.bfloat16)
    total = (
        jnp.einsum("lrk,lkp->lrp", local_field, basis, preferred_element_type=jnp.float32)
        + near_part
    )
    return total.astype(jnp.bfloat16)


def solution(mesh):
    assert tuple(mesh.shape.values()) == (64, 4)
    grid = Mesh(mesh.devices.reshape(8, 4, 2, 2, 2), ALL)
    return jax.shard_map(
        body,
        mesh=grid,
        in_specs=(
            P(ALL, None, None),
            P(ALL, None, None),
            P(ALL, None),
            P(ALL, None, None, None),
            P(ALL, None),
            P(ALL, None, None),
            P(ALL, None, None),
            P(ALL, None),
            P(ALL, None, None),
        ),
        out_specs=P(ALL, None, None),
        check_vma=False,
    )
```
